256 devices in a mesh: group: 16 (over x_lo, y, core), tensor: 16 (over z, x_hi).
Axes of the slice: x: 4 (x_hi: 2, x_lo: 2; x = x_hi * 2 + x_lo), y: 4, z: 8, core: 2. Of those that a mesh axis runs over, the one named last changes fastest.
Arguments:
- attention: bfloat16 [6144, 8192], P('group', 'tensor'), may hold values from -6 to 6
- out_weight: bfloat16 [8192, 8192], P('tensor', 'group'), may hold values from -0.0625 to 0.0625
- residual: bfloat16 [6144, 8192], P('group', 'tensor')
- gain: float32 [8192], P('tensor'), may hold values from 0.25 to 1.75
- token_tr: int32 [16, 384], P('group'), may hold values from 0 to 95, never falling along the last dimension, each value on 1 to 8 neighbouring positions
- lag_offsets: int32 [4], replicated, may hold values from 1 to 4, as said below
- responses: bfloat16 [1536, 10240], P(None, 'group'), may hold values from -6 to 6
Outputs:
- cross: float32 [4, 8192, 10240], P(None, 'tensor', 'group')
The draws below stay inside these ranges and needn't reach their ends.
Inputs may be any that keep to these rules, and one draw needn't show every extreme that they name: `token_tr`: within each group the TR numbers never fall, and every TR of the group holds 1 to 8 tokens. `lag_offsets`: the lags are the numbers 1 to 4 in some order.
All inputs are finite; a program needn't handle non-finite values.
Results may differ from the reference program's by a relative error of at most 0.0038.
Values may be sent and summed in bfloat16 or wider, within the bound.
No kernel may reach another device: no remote copies, remote signals or barrier semaphores. Data moves between devices by JAX's collectives and lax.ppermute only.
A program may use at most 128 MiB of HBM per device.

```python
import math
import jax
import jax.numpy as jnp
import numpy as np
from jax import lax

D = 8192
HEADS = 64
HD = 128
VOX = 10240
LAGS = 4
TR_MOST = 8
TOK_DEV = 384
R_DEV = 96
GROUPS = 16
TOKENS = 6144
TRS = 1536


def draw_residual(key, part):
    column = jnp.arange(D, dtype=jnp.float32) / (D - 1)
    values = jax.random.normal(jax.random.fold_in(key, 11), (TOKENS, D), jnp.float32)
    return (values * (3.0 ** column)[None, :]).astype(jnp.bfloat16)


def draw_lag_offsets(key, part):
    return (jax.random.permutation(jax.random.fold_in(key, 21), LAGS) + 1).astype(jnp.int32)


def shard_levels(own_key, dims, shards, low, top_value):
    def one(position, parts):
        steps = jax.random.uniform(jax.random.fold_in(jax.random.fold_in(own_key, 6), position), (parts,), jnp.float32, low / len(shards), top_value / len(shards))
        return jnp.repeat(jnp.exp(steps), dims[position] // parts).reshape((-1,) + (1,) * (len(dims) - position - 1))

    level = one(*shards[0])
    for cut in shards[1:]:
        level = level * one(*cut)
    return level


def length_profile(number_of, total, reach, slope):
    loads = [(1 << 20) // math.isqrt(standing ** slope) + 1 for standing in range(2, number_of + 1)]
    rest, given = total - reach - (number_of - 1), [1] * (number_of - 1)
    while rest > 0:
        candidates = [i for i in range(number_of - 1) if given[i] < reach]
        pool, remaining = sum([loads[i] for i in candidates]), rest
        for i in candidates:
            extra = min(reach - given[i], max(1, remaining * loads[i] // pool), rest)
            given[i] = given[i] + extra
            rest = rest - extra
    return np.array([reach] + given)


def ragged(key, number_of, total, most, slope):
    if number_of == 2:
        one = jax.random.randint(key, (), max(1, total - most), min(most, total - 1) + 1)
        return jnp.stack([one, total - one])
    lengths = jnp.asarray(length_profile(number_of, total, most, slope), jnp.int32)
    twos = (number_of - 1) // 2
    giver, taker = lengths[1:1 + 2 * twos:2], lengths[2:2 + 2 * twos:2]
    slack = jnp.minimum(giver - 1, most - taker)
    shifted = jax.random.randint(jax.random.fold_in(key, 1), (twos,), 0, 1 << 20) % (slack + 1)
    lengths = lengths.at[1:1 + 2 * twos:2].set(giver - shifted).at[2:2 + 2 * twos:2].set(taker + shifted)
    return lengths[jax.random.permutation(jax.random.fold_in(key, 2), number_of)]


def bell_draw(stream_key, shape, deviation, bound, split=(), kind=jnp.bfloat16):
    level = shard_levels(stream_key, shape, split, -0.22, 0.18) if split else 1.0
    result = jax.random.normal(stream_key, shape, jnp.float32) * deviation * level
    return jnp.minimum(jnp.maximum(result, -bound), bound).astype(kind)


def setup_inputs(seed: int = 0) -> dict:
    splits = jax.random.split(jax.random.key(seed), 8)
    attention = bell_draw(splits[0], (TOKENS, HEADS * HD), 1.0, 6.0, ((0, 16), (1, 16)))
    out_weight = bell_draw(splits[1], (HEADS * HD, D), (HEADS * HD) ** -0.5, 0.0625, ((0, 16), (1, 16)))
    residual = draw_residual(jax.random.fold_in(splits[7], 71), 0)
    gain = jnp.clip(1.0 + 0.15 * jax.random.normal(splits[3], (D,), jnp.float32), 0.25, 1.75)
    token_tr = jax.vmap(lambda own: jnp.searchsorted(jnp.cumsum(ragged(own, R_DEV, TOK_DEV, TR_MOST, 1)), jnp.arange(TOK_DEV), side="right"))(jax.random.split(splits[4], GROUPS)).reshape((GROUPS, TOK_DEV)).astype(jnp.int32)
    lag_offsets = draw_lag_offsets(jax.random.fold_in(splits[7], 71), 0)
    responses = bell_draw(splits[6], (TRS, VOX), 1.0, 6.0, ((1, 16),))
    return dict(attention=attention, out_weight=out_weight, residual=residual, gain=gain, token_tr=token_tr, lag_offsets=lag_offsets, responses=responses)


def reference(attention, out_weight, residual, gain, token_tr, lag_offsets, responses):
    mixed = jnp.dot(attention, out_weight, preferred_element_type=jnp.float32)
    hidden = residual.astype(jnp.float32) + mixed
    meansq = lax.optimization_barrier(jnp.mean(hidden * hidden, axis=1, keepdims=True))
    normed = (hidden * lax.rsqrt(meansq + 1e-05) * gain[None, :]).astype(jnp.bfloat16)
    group_ids = jnp.arange(token_tr.shape[0], dtype=jnp.int32)
    story_tr = (token_tr + group_ids[:, None] * R_DEV).reshape(-1)
    member = jnp.arange(TRS, dtype=jnp.int32)[:, None] == story_tr[None, :]
    counts = lax.optimization_barrier(jnp.sum(member.astype(jnp.float32), axis=1, keepdims=True))
    binned = (jnp.dot(member.astype(jnp.bfloat16), normed, preferred_element_type=jnp.float32) / counts).astype(jnp.bfloat16)
    rows_all = jnp.arange(TRS, dtype=jnp.int32)
    pieces = []
    for step in range(LAGS):
        source = rows_all - lag_offsets[step]
        valid = source >= 0
        taken = binned[jnp.maximum(source, 0)]
        pieces.append(jnp.where(valid[:, None], taken, jnp.zeros_like(taken)))
    lagged = jnp.stack(pieces, axis=1)
    cross = jnp.einsum('tld,tv->ldv', lagged.astype(jnp.float32), responses.astype(jnp.float32))
    return cross * (1.0 / jnp.sqrt(jnp.float32(TRS)))
```

```python
import jax
import jax.numpy as jnp
from jax import lax
from jax.sharding import PartitionSpec as P

D = 8192
LAGS = 4
R_DEV = 96


def transposed_block(block):
    groups = lax.axis_size("group")
    tensors = lax.axis_size("tensor")
    route = [(t * tensors + g, g * tensors + t) for g in range(groups) for t in range(tensors)]
    return lax.ppermute(block, ("group", "tensor"), route)


def on_device(attention, out_weight, residual, gain, token_tr, lag_offsets, responses):
    weight_cols = lax.all_gather(transposed_block(out_weight), "group", axis=0, tiled=True)
    rows = lax.all_gather(attention, "tensor", axis=1, tiled=True)
    summed = jnp.dot(rows, weight_cols, preferred_element_type=jnp.float32)
    hidden = residual.astype(jnp.float32) + summed
    squares = lax.psum(jnp.sum(hidden * hidden, axis=1), "tensor")
    normed = (hidden * lax.rsqrt(squares[:, None] / D + 1e-05) * gain[None, :]).astype(jnp.bfloat16)
    member = jnp.arange(R_DEV, dtype=jnp.int32)[:, None] == token_tr[0][None, :]
    counts = jnp.sum(member.astype(jnp.float32), axis=1, keepdims=True)
    binned = (
        jnp.dot(member.astype(jnp.bfloat16), normed, preferred_element_type=jnp.float32) / counts
    ).astype(jnp.bfloat16)
    width = binned.shape[1]
    total_trs = responses.shape[0]
    story = lax.all_gather(binned, "group", axis=0, tiled=True)
    extended = jnp.concatenate([jnp.zeros((LAGS, width), story.dtype), story], axis=0)
    pieces = []
    for step in range(LAGS):
        start = LAGS - lag_offsets[step]
        pieces.append(lax.dynamic_slice_in_dim(extended, start, total_trs, 0))
    lagged = jnp.concatenate(pieces, axis=1)
    contract = (((0,), (0,)), ((), ()))
    accumulated = lax.dot_general(lagged, responses, contract, preferred_element_type=jnp.float32)
    scaled = accumulated * (1.0 / jnp.sqrt(jnp.float32(total_trs)))
    return scaled.reshape(LAGS, width, responses.shape[1])


def solution(mesh):
    return jax.shard_map(
        on_device,
        mesh=mesh,
        in_specs=(
            P("group", "tensor"),
            P("tensor", "group"),
            P("group", "tensor"),
            P("tensor"),
            P("group", None),
            P(),
            P(None, "group"),
        ),
        out_specs=P(None, "tensor", "group"),
        check_vma=False,
    )
```

```python
import jax
import jax.numpy as jnp
from jax import lax
from jax.sharding import PartitionSpec as P

D = 8192
LAGS = 4
R_DEV = 96


def transposed_block(block):
    groups = lax.axis_size("group")
    tensors = lax.axis_size("tensor")
    route = [(t * tensors + g, g * tensors + t) for g in range(groups) for t in range(tensors)]
    return lax.ppermute(block, ("group", "tensor"), route)


def shifted(block, axis, shift):
    n = lax.axis_size(axis)
    return lax.ppermute(block, axis, [(i, (i + shift) % n) for i in range(n)])


def gathered_by_shift(block, axis):
    n = lax.axis_size(axis)
    return [block] + [shifted(block, axis, k) for k in range(1, n)]


def on_device(attention, out_weight, residual, gain, token_tr, lag_offsets, responses):
    tensors = lax.axis_size("tensor")
    own = lax.axis_index("tensor")
    heads = attention.shape[1]
    weight_cols = lax.all_gather(transposed_block(out_weight), "group", axis=0, tiled=True)
    rows = jnp.concatenate(gathered_by_shift(attention, "tensor"), axis=1)
    flipped = weight_cols.reshape(tensors, heads, -1)[::-1]
    doubled = jnp.concatenate([flipped, flipped], axis=0)
    reordered = lax.dynamic_slice_in_dim(doubled, tensors - 1 - own, tensors, 0)
    summed = jnp.dot(rows, reordered.reshape(tensors * heads, -1), preferred_element_type=jnp.float32)
    hidden = residual.astype(jnp.float32) + summed
    partial = jnp.sum(hidden * hidden, axis=1)
    squares = sum(gathered_by_shift(partial, "tensor"))
    normed = (hidden * lax.rsqrt(squares[:, None] / D + 1e-05) * gain[None, :]).astype(jnp.bfloat16)
    member = jnp.arange(R_DEV, dtype=jnp.int32)[:, None] == token_tr[0][None, :]
    counts = jnp.sum(member.astype(jnp.float32), axis=1, keepdims=True)
    binned = (
        jnp.dot(member.astype(jnp.bfloat16), normed, preferred_element_type=jnp.float32) / counts
    ).astype(jnp.bfloat16)
    width = binned.shape[1]
    total_trs = responses.shape[0]
    story = lax.all_gather(binned, "group", axis=0, tiled=True)
    extended = jnp.concatenate([jnp.zeros((LAGS, width), story.dtype), story], axis=0)
    pieces = []
    for step in range(LAGS):
        start = LAGS - lag_offsets[step]
        pieces.append(lax.dynamic_slice_in_dim(extended, start, total_trs, 0))
    lagged = jnp.concatenate(pieces, axis=1)
    contract = (((0,), (0,)), ((), ()))
    accumulated = lax.dot_general(lagged, responses, contract, preferred_element_type=jnp.float32)
    scaled = accumulated * (1.0 / jnp.sqrt(jnp.float32(total_trs)))
    return scaled.reshape(LAGS, width, responses.shape[1])


def solution(mesh):
    return jax.shard_map(
        on_device,
        mesh=mesh,
        in_specs=(
            P("group", "tensor"),
            P("tensor", "group"),
            P("group", "tensor"),
            P("tensor"),
            P("group", None),
            P(),
            P(None, "group"),
        ),
        out_specs=P(None, "tensor", "group"),
        check_vma=False,
    )
```

```python
import jax
import jax.numpy as jnp
from jax import lax
from jax.sharding import Mesh, PartitionSpec as P

D = 8192
LAGS = 4
R_DEV = 96
GROUP = ("xlo", "y", "core")
TENSOR = ("z", "xhi")


def transposed_block(block):
    groups = lax.axis_size(GROUP)
    tensors = lax.axis_size(TENSOR)
    route = [(t * tensors + g, g * tensors + t) for g in range(groups) for t in range(tensors)]
    return lax.ppermute(block, GROUP + TENSOR, route)


def on_device(attention, out_weight, residual, gain, token_tr, lag_offsets, responses):
    weight_cols = lax.all_gather(transposed_block(out_weight), GROUP, axis=0, tiled=True)
    rows = lax.all_gather(lax.all_gather(attention, "xhi", axis=1, tiled=True), "z", axis=1, tiled=True)
    summed = jnp.dot(rows, weight_cols, preferred_element_type=jnp.float32)
    hidden = residual.astype(jnp.float32) + summed
    squares = lax.psum(lax.psum(jnp.sum(hidden * hidden, axis=1), "xhi"), "z")
    normed = (hidden * lax.rsqrt(squares[:, None] / D + 1e-05) * gain[None, :]).astype(jnp.bfloat16)
    member = jnp.arange(R_DEV, dtype=jnp.int32)[:, None] == token_tr[0][None, :]
    counts = jnp.sum(member.astype(jnp.float32), axis=1, keepdims=True)
    binned = (
        jnp.dot(member.astype(jnp.bfloat16), normed, preferred_element_type=jnp.float32) / counts
    ).astype(jnp.bfloat16)
    width = binned.shape[1]
    total_trs = responses.shape[0]
    story = lax.all_gather(binned, GROUP, axis=0, tiled=True)
    extended = jnp.concatenate([jnp.zeros((LAGS, width), story.dtype), story], axis=0)
    pieces = []
    for step in range(LAGS):
        start = LAGS - lag_offsets[step]
        pieces.append(lax.dynamic_slice_in_dim(extended, start, total_trs, 0))
    lagged = jnp.concatenate(pieces, axis=1)
    contract = (((0,), (0,)), ((), ()))
    accumulated = lax.dot_general(lagged, responses, contract, preferred_element_type=jnp.float32)
    scaled = accumulated * (1.0 / jnp.sqrt(jnp.float32(total_trs)))
    return scaled.reshape(LAGS, width, responses.shape[1])


def solution(mesh):
    parts = Mesh(mesh.devices.reshape(2, 4, 2, 8, 2), GROUP + TENSOR)
    return jax.shard_map(
        on_device,
        mesh=parts,
        in_specs=(
            P(GROUP, TENSOR),
            P(TENSOR, GROUP),
            P(GROUP, TENSOR),
            P(TENSOR),
            P(GROUP, None),
            P(),
            P(None, GROUP),
        ),
        out_specs=P(None, TENSOR, GROUP),
        check_vma=False,
    )
```

```python
import jax
import jax.numpy as jnp
from jax import lax
from jax.sharding import Mesh, PartitionSpec as P

D = 8192
LAGS = 4
R_DEV = 96
GROUP = ("xlo", "y", "core")
TENSOR = ("z", "xhi")


def core_last(g, cores, rest):
    return (g % cores) * rest + g // cores


def transposed_block(block):
    groups = lax.axis_size(GROUP)
    tensors = lax.axis_size(TENSOR)
    cores = lax.axis_size("core")
    route = [
        (t * tensors + core_last(g, cores, groups // cores), g * tensors + t)
        for g in range(groups)
        for t in range(tensors)
    ]
    return lax.ppermute(block, GROUP + TENSOR, route)


def gather_core_last(block, axis):
    return lax.all_gather(lax.all_gather(block, GROUP[:-1], axis=axis, tiled=True), "core", axis=axis, tiled=True)


def on_device(attention, out_weight, residual, gain, token_tr, lag_offsets, responses):
    weight_cols = gather_core_last(transposed_block(out_weight), 0)
    rows = lax.all_gather(lax.all_gather(attention, "xhi", axis=1, tiled=True), "z", axis=1, tiled=True)
    summed = jnp.dot(rows, weight_cols, preferred_element_type=jnp.float32)
    hidden = residual.astype(jnp.float32) + summed
    squares = lax.psum(lax.psum(jnp.sum(hidden * hidden, axis=1), "xhi"), "z")
    normed = (hidden * lax.rsqrt(squares[:, None] / D + 1e-05) * gain[None, :]).astype(jnp.bfloat16)
    member = jnp.arange(R_DEV, dtype=jnp.int32)[:, None] == token_tr[0][None, :]
    counts = jnp.sum(member.astype(jnp.float32), axis=1, keepdims=True)
    binned = (
        jnp.dot(member.astype(jnp.bfloat16), normed, preferred_element_type=jnp.float32) / counts
    ).astype(jnp.bfloat16)
    width = binned.shape[1]
    total_trs = responses.shape[0]
    by_core = lax.all_gather(lax.all_gather(binned, GROUP[:-1], axis=0), "core", axis=0)
    story = jnp.swapaxes(by_core, 0, 1).reshape(-1, width)
    extended = jnp.concatenate([jnp.zeros((LAGS, width), story.dtype), story], axis=0)
    pieces = []
    for step in range(LAGS):
        start = LAGS - lag_offsets[step]
        pieces.append(lax.dynamic_slice_in_dim(extended, start, total_trs, 0))
    lagged = jnp.concatenate(pieces, axis=1)
    contract = (((0,), (0,)), ((), ()))
    accumulated = lax.dot_general(lagged, responses, contract, preferred_element_type=jnp.float32)
    scaled = accumulated * (1.0 / jnp.sqrt(jnp.float32(total_trs)))
    return scaled.reshape(LAGS, width, responses.shape[1])


def solution(mesh):
    parts = Mesh(mesh.devices.reshape(2, 4, 2, 8, 2), GROUP + TENSOR)
    return jax.shard_map(
        on_device,
        mesh=parts,
        in_specs=(
            P(GROUP, TENSOR),
            P(TENSOR, GROUP),
            P(GROUP, TENSOR),
            P(TENSOR),
            P(GROUP, None),
            P(),
            P(None, GROUP),
        ),
        out_specs=P(None, TENSOR, GROUP),
        check_vma=False,
    )
```

```python
import jax
import jax.numpy as jnp
from jax import lax
from jax.sharding import Mesh, PartitionSpec as P

D = 8192
LAGS = 4
R_DEV = 96
GROUP = ("xlo", "y", "core")
TENSOR = ("z", "xhi")


def z_ring_block(block):
    groups = lax.axis_size(GROUP)
    tensors = lax.axis_size(TENSOR)
    xs = lax.axis_size("xhi")
    route = []
    for g in range(groups):
        for t in range(tensors):
            z, x = t // xs, t % xs
            source = (xs * (g // xs) + x) * tensors + xs * z + g % xs
            route.append((source, g * tensors + t))
    return lax.ppermute(block, GROUP + TENSOR, route)


def on_device(attention, out_weight, residual, gain, token_tr, lag_offsets, responses):
    xs = lax.axis_size("xhi")
    zs = lax.axis_size("z")
    heads = attention.shape[1]
    slab = lax.all_gather(attention, "xhi", axis=1, tiled=True)
    blocks = lax.all_gather(z_ring_block(out_weight), GROUP, axis=0).reshape(zs, xs, heads, -1)
    partial = jnp.einsum(
        "ich,zchf->izf", slab.reshape(-1, xs, heads), blocks, preferred_element_type=jnp.float32
    )
    received = lax.all_to_all(partial.astype(jnp.bfloat16), "z", 1, 1, tiled=True)
    summed = jnp.sum(received.astype(jnp.float32), axis=1)
    hidden = residual.astype(jnp.float32) + summed
    squares = lax.psum(lax.psum(jnp.sum(hidden * hidden, axis=1), "xhi"), "z")
    normed = (hidden * lax.rsqrt(squares[:, None] / D + 1e-05) * gain[None, :]).astype(jnp.bfloat16)
    member = jnp.arange(R_DEV, dtype=jnp.int32)[:, None] == token_tr[0][None, :]
    counts = jnp.sum(member.astype(jnp.float32), axis=1, keepdims=True)
    binned = (
        jnp.dot(member.astype(jnp.bfloat16), normed, preferred_element_type=jnp.float32) / counts
    ).astype(jnp.bfloat16)
    width = binned.shape[1]
    total_trs = responses.shape[0]
    story = lax.all_gather(binned, GROUP, axis=0, tiled=True)
    extended = jnp.concatenate([jnp.zeros((LAGS, width), story.dtype), story], axis=0)
    pieces = []
    for step in range(LAGS):
        start = LAGS - lag_offsets[step]
        pieces.append(lax.dynamic_slice_in_dim(extended, start, total_trs, 0))
    lagged = jnp.concatenate(pieces, axis=1)
    contract = (((0,), (0,)), ((), ()))
    accumulated = lax.dot_general(lagged, responses, contract, preferred_element_type=jnp.float32)
    scaled = accumulated * (1.0 / jnp.sqrt(jnp.float32(total_trs)))
    return scaled.reshape(LAGS, width, responses.shape[1])


def solution(mesh):
    parts = Mesh(mesh.devices.reshape(2, 4, 2, 8, 2), GROUP + TENSOR)
    return jax.shard_map(
        on_device,
        mesh=parts,
        in_specs=(
            P(GROUP, TENSOR),
            P(TENSOR, GROUP),
            P(GROUP, TENSOR),
            P(TENSOR),
            P(GROUP, None),
            P(),
            P(None, GROUP),
        ),
        out_specs=P(None, TENSOR, GROUP),
        check_vma=False,
    )
```

```python
import jax
import jax.numpy as jnp
from jax import lax
from jax.sharding import Mesh, PartitionSpec as P

D = 8192
LAGS = 4
R_DEV = 96
GROUP = ("xlo", "y", "core")
TENSOR = ("z", "xhi")


def z_ring_block(block):
    groups = lax.axis_size(GROUP)
    tensors = lax.axis_size(TENSOR)
    xs = lax.axis_size("xhi")
    route = []
    for g in range(groups):
        for t in range(tensors):
            z, x = t // xs, t % xs
            source = (xs * (g // xs) + x) * tensors + xs * z + g % xs
            route.append((source, g * tensors + t))
    return lax.ppermute(block, GROUP + TENSOR, route)


def on_device(attention, out_weight, residual, gain, token_tr, lag_offsets, responses):
    xs = lax.axis_size("xhi")
    zs = lax.axis_size("z")
    heads = attention.shape[1]
    slab = lax.all_gather(attention, "xhi", axis=1, tiled=True)
    blocks = lax.all_gather(z_ring_block(out_weight), GROUP, axis=0).reshape(zs, xs, heads, -1)
    partial = jnp.einsum(
        "ich,zchf->izf", slab.reshape(-1, xs, heads), blocks, preferred_element_type=jnp.float32
    )
    received = lax.all_to_all(partial.astype(jnp.bfloat16), "z", 1, 1, tiled=True)
    summed = jnp.sum(received.astype(jnp.float32), axis=1)
    hidden = residual.astype(jnp.float32) + summed
    squares = jnp.sum(lax.all_gather(jnp.sum(hidden * hidden, axis=1), TENSOR, axis=0), axis=0)
    normed = (hidden * lax.rsqrt(squares[:, None] / D + 1e-05) * gain[None, :]).astype(jnp.bfloat16)
    member = jnp.arange(R_DEV, dtype=jnp.int32)[:, None] == token_tr[0][None, :]
    counts = jnp.sum(member.astype(jnp.float32), axis=1, keepdims=True)
    binned = (
        jnp.dot(member.astype(jnp.bfloat16), normed, preferred_element_type=jnp.float32) / counts
    ).astype(jnp.bfloat16)
    width = binned.shape[1]
    total_trs = responses.shape[0]
    story = lax.all_gather(binned, GROUP, axis=0, tiled=True)
    extended = jnp.concatenate([jnp.zeros((LAGS, width), story.dtype), story], axis=0)
    pieces = []
    for step in range(LAGS):
        start = LAGS - lag_offsets[step]
        pieces.append(lax.dynamic_slice_in_dim(extended, start, total_trs, 0))
    lagged = jnp.concatenate(pieces, axis=1)
    contract = (((0,), (0,)), ((), ()))
    accumulated = lax.dot_general(lagged, responses, contract, preferred_element_type=jnp.float32)
    scaled = accumulated * (1.0 / jnp.sqrt(jnp.float32(total_trs)))
    return scaled.reshape(LAGS, width, responses.shape[1])


def solution(mesh):
    parts = Mesh(mesh.devices.reshape(2, 4, 2, 8, 2), GROUP + TENSOR)
    return jax.shard_map(
        on_device,
        mesh=parts,
        in_specs=(
            P(GROUP, TENSOR),
            P(TENSOR, GROUP),
            P(GROUP, TENSOR),
            P(TENSOR),
            P(GROUP, None),
            P(),
            P(None, GROUP),
        ),
        out_specs=P(None, TENSOR, GROUP),
        check_vma=False,
    )
```

```python
import jax
import jax.numpy as jnp
from jax import lax
from jax.sharding import Mesh, PartitionSpec as P

D = 8192
LAGS = 4
R_DEV = 96
GROUP = ("xlo", "y", "core")
TENSOR = ("zhi", "zlo", "xhi")


def ring_block(block):
    groups = lax.axis_size(GROUP)
    tensors = lax.axis_size(TENSOR)
    quad = lax.axis_size(("zlo", "xhi"))
    route = []
    for g in range(groups):
        for t in range(tensors):
            ring, q = t // quad, t % quad
            source = (quad * (g // quad) + q) * tensors + quad * ring + g % quad
            route.append((source, g * tensors + t))
    return lax.ppermute(block, GROUP + TENSOR, route)


def on_device(attention, out_weight, residual, gain, token_tr, lag_offsets, responses):
    quad = lax.axis_size(("zlo", "xhi"))
    ring = lax.axis_size("zhi")
    heads = attention.shape[1]
    slab = lax.all_gather(attention, ("zlo", "xhi"), axis=1, tiled=True)
    blocks = lax.all_gather(ring_block(out_weight), GROUP, axis=0).reshape(ring, quad, heads, -1)
    partial = jnp.einsum(
        "iqh,rqhf->irf", slab.reshape(-1, quad, heads), blocks, preferred_element_type=jnp.float32
    )
    received = lax.all_to_all(partial.astype(jnp.bfloat16), "zhi", 1, 1, tiled=True)
    summed = jnp.sum(received.astype(jnp.float32), axis=1)
    hidden = residual.astype(jnp.float32) + summed
    squares = lax.psum(lax.psum(jnp.sum(hidden * hidden, axis=1), "xhi"), ("zhi", "zlo"))
    normed = (hidden * lax.rsqrt(squares[:, None] / D + 1e-05) * gain[None, :]).astype(jnp.bfloat16)
    member = jnp.arange(R_DEV, dtype=jnp.int32)[:, None] == token_tr[0][None, :]
    counts = jnp.sum(member.astype(jnp.float32), axis=1, keepdims=True)
    binned = (
        jnp.dot(member.astype(jnp.bfloat16), normed, preferred_element_type=jnp.float32) / counts
    ).astype(jnp.bfloat16)
    width = binned.shape[1]
    total_trs = responses.shape[0]
    story = lax.all_gather(binned, GROUP, axis=0, tiled=True)
    extended = jnp.concatenate([jnp.zeros((LAGS, width), story.dtype), story], axis=0)
    pieces = []
    for step in range(LAGS):
        start = LAGS - lag_offsets[step]
        pieces.append(lax.dynamic_slice_in_dim(extended, start, total_trs, 0))
    lagged = jnp.concatenate(pieces, axis=1)
    contract = (((0,), (0,)), ((), ()))
    accumulated = lax.dot_general(lagged, responses, contract, preferred_element_type=jnp.float32)
    scaled = accumulated * (1.0 / jnp.sqrt(jnp.float32(total_trs)))
    return scaled.reshape(LAGS, width, responses.shape[1])


def solution(mesh):
    parts = Mesh(mesh.devices.reshape(2, 4, 2, 4, 2, 2), GROUP + TENSOR)
    return jax.shard_map(
        on_device,
        mesh=parts,
        in_specs=(
            P(GROUP, TENSOR),
            P(TENSOR, GROUP),
            P(GROUP, TENSOR),
            P(TENSOR),
            P(GROUP, None),
            P(),
            P(None, GROUP),
        ),
        out_specs=P(None, TENSOR, GROUP),
        check_vma=False,
    )
```

```python
import jax
import jax.numpy as jnp
from jax import lax
from jax.sharding import Mesh, PartitionSpec as P

D = 8192
LAGS = 4
R_DEV = 96
GROUP = ("xlo", "y", "core")
TENSOR = ("zhi", "zlo", "xhi")


def ring_block(block):
    groups = lax.axis_size(GROUP)
    tensors = lax.axis_size(TENSOR)
    quad = lax.axis_size(("zlo", "xhi"))
    route = []
    for g in range(groups):
        for t in range(tensors):
            ring, q = t // quad, t % quad
            source = (quad * (g // quad) + q) * tensors + quad * ring + g % quad
            route.append((source, g * tensors + t))
    return lax.ppermute(block, GROUP + TENSOR, route)


def on_device(attention, out_weight, residual, gain, token_tr, lag_offsets, responses):
    quad = lax.axis_size(("zlo", "xhi"))
    ring = lax.axis_size("zhi")
    heads = attention.shape[1]
    pair = lax.all_gather(attention, "xhi", axis=1, tiled=True)
    other = lax.ppermute(pair, "zlo", [(0, 1), (1, 0)])
    low = lax.axis_index("zlo") == 0
    slab = jnp.concatenate([jnp.where(low, pair, other), jnp.where(low, other, pair)], axis=1)
    blocks = lax.all_gather(ring_block(out_weight), GROUP, axis=0).reshape(ring, quad, heads, -1)
    partial = jnp.einsum(
        "iqh,rqhf->irf", slab.reshape(-1, quad, heads), blocks, preferred_element_type=jnp.float32
    )
    received = lax.all_to_all(partial.astype(jnp.bfloat16), "zhi", 1, 1, tiled=True)
    summed = jnp.sum(received.astype(jnp.float32), axis=1)
    hidden = residual.astype(jnp.float32) + summed
    squares = lax.psum(lax.psum(jnp.sum(hidden * hidden, axis=1), "xhi"), ("zhi", "zlo"))
    normed = (hidden * lax.rsqrt(squares[:, None] / D + 1e-05) * gain[None, :]).astype(jnp.bfloat16)
    member = jnp.arange(R_DEV, dtype=jnp.int32)[:, None] == token_tr[0][None, :]
    counts = jnp.sum(member.astype(jnp.float32), axis=1, keepdims=True)
    binned = (
        jnp.dot(member.astype(jnp.bfloat16), normed, preferred_element_type=jnp.float32) / counts
    ).astype(jnp.bfloat16)
    width = binned.shape[1]
    total_trs = responses.shape[0]
    story = lax.all_gather(binned, GROUP, axis=0, tiled=True)
    extended = jnp.concatenate([jnp.zeros((LAGS, width), story.dtype), story], axis=0)
    pieces = []
    for step in range(LAGS):
        start = LAGS - lag_offsets[step]
        pieces.append(lax.dynamic_slice_in_dim(extended, start, total_trs, 0))
    lagged = jnp.concatenate(pieces, axis=1)
    contract = (((0,), (0,)), ((), ()))
    accumulated = lax.dot_general(lagged, responses, contract, preferred_element_type=jnp.float32)
    scaled = accumulated * (1.0 / jnp.sqrt(jnp.float32(total_trs)))
    return scaled.reshape(LAGS, width, responses.shape[1])


def solution(mesh):
    parts = Mesh(mesh.devices.reshape(2, 4, 2, 4, 2, 2), GROUP + TENSOR)
    return jax.shard_map(
        on_device,
        mesh=parts,
        in_specs=(
            P(GROUP, TENSOR),
            P(TENSOR, GROUP),
            P(GROUP, TENSOR),
            P(TENSOR),
            P(GROUP, None),
            P(),
            P(None, GROUP),
        ),
        out_specs=P(None, TENSOR, GROUP),
        check_vma=False,
    )
```

```python
import jax
import jax.numpy as jnp
from jax import lax
from jax.sharding import Mesh, PartitionSpec as P

D = 8192
LAGS = 4
R_DEV = 96
GROUP = ("xlo", "y", "core")
TENSOR = ("zhi", "zlo", "xhi")


def ring_block(block):
    groups = lax.axis_size(GROUP)
    tensors = lax.axis_size(TENSOR)
    quad = lax.axis_size(("zlo", "xhi"))
    route = []
    for g in range(groups):
        for t in range(tensors):
            ring, q = t // quad, t % quad
            source = (quad * (g // quad) + q) * tensors + quad * ring + g % quad
            route.append((source, g * tensors + t))
    return lax.ppermute(block, GROUP + TENSOR, route)


def on_device(attention, out_weight, residual, gain, token_tr, lag_offsets, responses):
    quad = lax.axis_size(("zlo", "xhi"))
    ring = lax.axis_size("zhi")
    heads = attention.shape[1]
    pair = lax.all_gather(attention, "xhi", axis=1, tiled=True)
    other = lax.ppermute(pair, "zlo", [(0, 1), (1, 0)])
    low = lax.axis_index("zlo") == 0
    slab = jnp.concatenate([jnp.where(low, pair, other), jnp.where(low, other, pair)], axis=1)
    blocks = lax.all_gather(ring_block(out_weight), GROUP, axis=0).reshape(ring, quad, heads, -1)
    partial = jnp.einsum(
        "iqh,rqhf->irf", slab.reshape(-1, quad, heads), blocks, preferred_element_type=jnp.float32
    )
    received = lax.all_to_all(partial.astype(jnp.bfloat16), "zhi", 1, 1, tiled=True)
    summed = jnp.sum(received.astype(jnp.float32), axis=1)
    hidden = residual.astype(jnp.float32) + summed
    squares = jnp.sum(hidden * hidden, axis=1)
    for axis, mask in (("xhi", 1), ("zlo", 1), ("zhi", 1), ("zhi", 2)):
        size = lax.axis_size(axis)
        squares = squares + lax.ppermute(squares, axis, [(i, i ^ mask) for i in range(size)])
    normed = (hidden * lax.rsqrt(squares[:, None] / D + 1e-05) * gain[None, :]).astype(jnp.bfloat16)
    member = jnp.arange(R_DEV, dtype=jnp.int32)[:, None] == token_tr[0][None, :]
    counts = jnp.sum(member.astype(jnp.float32), axis=1, keepdims=True)
    binned = (
        jnp.dot(member.astype(jnp.bfloat16), normed, preferred_element_type=jnp.float32) / counts
    ).astype(jnp.bfloat16)
    width = binned.shape[1]
    total_trs = responses.shape[0]
    story = lax.all_gather(binned, GROUP, axis=0, tiled=True)
    extended = jnp.concatenate([jnp.zeros((LAGS, width), story.dtype), story], axis=0)
    pieces = []
    for step in range(LAGS):
        start = LAGS - lag_offsets[step]
        pieces.append(lax.dynamic_slice_in_dim(extended, start, total_trs, 0))
    lagged = jnp.concatenate(pieces, axis=1)
    contract = (((0,), (0,)), ((), ()))
    accumulated = lax.dot_general(lagged, responses, contract, preferred_element_type=jnp.float32)
    scaled = accumulated * (1.0 / jnp.sqrt(jnp.float32(total_trs)))
    return scaled.reshape(LAGS, width, responses.shape[1])


def solution(mesh):
    parts = Mesh(mesh.devices.reshape(2, 4, 2, 4, 2, 2), GROUP + TENSOR)
    return jax.shard_map(
        on_device,
        mesh=parts,
        in_specs=(
            P(GROUP, TENSOR),
            P(TENSOR, GROUP),
            P(GROUP, TENSOR),
            P(TENSOR),
            P(GROUP, None),
            P(),
            P(None, GROUP),
        ),
        out_specs=P(None, TENSOR, GROUP),
        check_vma=False,
    )
```

```python
import jax
import jax.numpy as jnp
from jax import lax
from jax.sharding import Mesh, PartitionSpec as P

D = 8192
LAGS = 4
R_DEV = 96
GROUP = ("xlo", "y", "core")
TENSOR = ("zhi", "zlo", "xhi")


def ring_block(block):
    groups = lax.axis_size(GROUP)
    tensors = lax.axis_size(TENSOR)
    quad = lax.axis_size(("zlo", "xhi"))
    route = []
    for g in range(groups):
        for t in range(tensors):
            ring, q = t // quad, t % quad
            source = (quad * (g // quad) + q) * tensors + quad * ring + g % quad
            route.append((source, g * tensors + t))
    return lax.ppermute(block, GROUP + TENSOR, route)


def on_device(attention, out_weight, residual, gain, token_tr, lag_offsets, responses):
    quad = lax.axis_size(("zlo", "xhi"))
    ring = lax.axis_size("zhi")
    heads = attention.shape[1]
    pair = lax.all_gather(attention, "xhi", axis=1, tiled=True)
    other = lax.ppermute(pair, "zlo", [(0, 1), (1, 0)])
    low = lax.axis_index("zlo") == 0
    slab = jnp.concatenate([jnp.where(low, pair, other), jnp.where(low, other, pair)], axis=1)
    blocks = lax.all_gather(ring_block(out_weight), GROUP, axis=0).reshape(ring, quad, heads, -1)
    partial = jnp.einsum(
        "iqh,rqhf->irf", slab.reshape(-1, quad, heads), blocks, preferred_element_type=jnp.float32
    )
    received = lax.all_to_all(partial.astype(jnp.bfloat16), "zhi", 1, 1, tiled=True)
    summed = jnp.sum(received.astype(jnp.float32), axis=1)
    hidden = residual.astype(jnp.float32) + summed
    squares = jnp.sum(hidden * hidden, axis=1)
    for axis, mask in (("xhi", 1), ("zlo", 1), ("zhi", 1), ("zhi", 2)):
        size = lax.axis_size(axis)
        squares = squares + lax.ppermute(squares, axis, [(i, i ^ mask) for i in range(size)])
    normed = (hidden * lax.rsqrt(squares[:, None] / D + 1e-05) * gain[None, :]).astype(jnp.bfloat16)
    member = jnp.arange(R_DEV, dtype=jnp.int32)[:, None] == token_tr[0][None, :]
    counts = jnp.sum(member.astype(jnp.float32), axis=1, keepdims=True)
    binned = (
        jnp.dot(member.astype(jnp.bfloat16), normed, preferred_element_type=jnp.float32) / counts
    ).astype(jnp.bfloat16)
    width = binned.shape[1]
    total_trs = responses.shape[0]
    story = lax.all_gather(binned, GROUP, axis=0, tiled=True)
    extended = jnp.concatenate([jnp.zeros((LAGS, width), story.dtype), story], axis=0)
    contract = (((0,), (0,)), ((), ()))
    products = []
    for step in range(LAGS):
        start = LAGS - lag_offsets[step]
        lagged = lax.dynamic_slice_in_dim(extended, start, total_trs, 0)
        products.append(lax.dot_general(lagged, responses, contract, preferred_element_type=jnp.float32))
    scaled = jnp.stack(products) * (1.0 / jnp.sqrt(jnp.float32(total_trs)))
    return scaled.reshape(LAGS, width, responses.shape[1])


def solution(mesh):
    parts = Mesh(mesh.devices.reshape(2, 4, 2, 4, 2, 2), GROUP + TENSOR)
    return jax.shard_map(
        on_device,
        mesh=parts,
        in_specs=(
            P(GROUP, TENSOR),
            P(TENSOR, GROUP),
            P(GROUP, TENSOR),
            P(TENSOR),
            P(GROUP, None),
            P(),
            P(None, GROUP),
        ),
        out_specs=P(None, TENSOR, GROUP),
        check_vma=False,
    )
```

```python
import jax
import jax.numpy as jnp
from jax import lax
from jax.sharding import Mesh, PartitionSpec as P

D = 8192
LAGS = 4
R_DEV = 96
GROUP = ("xlo", "y", "core")
TENSOR = ("zhi", "zlo", "xhi")


def ring_block(block):
    groups = lax.axis_size(GROUP)
    tensors = lax.axis_size(TENSOR)
    quad = lax.axis_size(("zlo", "xhi"))
    route = []
    for g in range(groups):
        for t in range(tensors):
            ring, q = t // quad, t % quad
            source = (quad * (g // quad) + q) * tensors + quad * ring + g % quad
            route.append((source, g * tensors + t))
    return lax.ppermute(block, GROUP + TENSOR, route)


def on_device(attention, out_weight, residual, gain, token_tr, lag_offsets, responses):
    quad = lax.axis_size(("zlo", "xhi"))
    ring = lax.axis_size("zhi")
    heads = attention.shape[1]
    pair = lax.all_gather(attention, "xhi", axis=1, tiled=True)
    other = lax.ppermute(pair, "zlo", [(0, 1), (1, 0)])
    low = lax.axis_index("zlo") == 0
    slab = jnp.concatenate([jnp.where(low, pair, other), jnp.where(low, other, pair)], axis=1)
    blocks = lax.all_gather(ring_block(out_weight), GROUP, axis=0).reshape(ring, quad, heads, -1)
    own = lax.axis_index("zhi")
    lhs = slab.reshape(-1, quad, heads)
    summed = None
    for shift in range(ring):
        cols = lax.dynamic_index_in_dim(blocks, (own + shift) % ring, 0, keepdims=False)
        part = jnp.einsum("iqh,qhf->if", lhs, cols, preferred_element_type=jnp.float32)
        if shift == 0:
            summed = part
        else:
            route = [(i, (i + shift) % ring) for i in range(ring)]
            summed = summed + lax.ppermute(part.astype(jnp.bfloat16), "zhi", route).astype(jnp.float32)
    hidden = residual.astype(jnp.float32) + summed
    squares = jnp.sum(hidden * hidden, axis=1)
    for axis, mask in (("xhi", 1), ("zlo", 1), ("zhi", 1), ("zhi", 2)):
        size = lax.axis_size(axis)
        squares = squares + lax.ppermute(squares, axis, [(i, i ^ mask) for i in range(size)])
    normed = (hidden * lax.rsqrt(squares[:, None] / D + 1e-05) * gain[None, :]).astype(jnp.bfloat16)
    member = jnp.arange(R_DEV, dtype=jnp.int32)[:, None] == token_tr[0][None, :]
    counts = jnp.sum(member.astype(jnp.float32), axis=1, keepdims=True)
    binned = (
        jnp.dot(member.astype(jnp.bfloat16), normed, preferred_element_type=jnp.float32) / counts
    ).astype(jnp.bfloat16)
    width = binned.shape[1]
    total_trs = responses.shape[0]
    story = lax.all_gather(binned, GROUP, axis=0, tiled=True)
    extended = jnp.concatenate([jnp.zeros((LAGS, width), story.dtype), story], axis=0)
    contract = (((0,), (0,)), ((), ()))
    products = []
    for step in range(LAGS):
        start = LAGS - lag_offsets[step]
        lagged = lax.dynamic_slice_in_dim(extended, start, total_trs, 0)
        products.append(lax.dot_general(lagged, responses, contract, preferred_element_type=jnp.float32))
    scaled = jnp.stack(products) * (1.0 / jnp.sqrt(jnp.float32(total_trs)))
    return scaled.reshape(LAGS, width, responses.shape[1])


def solution(mesh):
    parts = Mesh(mesh.devices.reshape(2, 4, 2, 4, 2, 2), GROUP + TENSOR)
    return jax.shard_map(
        on_device,
        mesh=parts,
        in_specs=(
            P(GROUP, TENSOR),
            P(TENSOR, GROUP),
            P(GROUP, TENSOR),
            P(TENSOR),
            P(GROUP, None),
            P(),
            P(None, GROUP),
        ),
        out_specs=P(None, TENSOR, GROUP),
        check_vma=False,
    )
```

```python
import jax
import jax.numpy as jnp
from jax import lax
from jax.sharding import Mesh, PartitionSpec as P

D = 8192
LAGS = 4
R_DEV = 96
GROUP = ("xlo", "y", "core")
TENSOR = ("zhi", "zlo", "xhi")


def ring_block(block):
    groups = lax.axis_size(GROUP)
    tensors = lax.axis_size(TENSOR)
    quad = lax.axis_size(("zlo", "xhi"))
    route = []
    for g in range(groups):
        for t in range(tensors):
            ring, q = t // quad, t % quad
            source = (quad * (g // quad) + q) * tensors + quad * ring + g % quad
            route.append((source, g * tensors + t))
    return lax.ppermute(block, GROUP + TENSOR, route)


def on_device(attention, out_weight, residual, gain, token_tr, lag_offsets, responses):
    quad = lax.axis_size(("zlo", "xhi"))
    ring = lax.axis_size("zhi")
    heads = attention.shape[1]
    quad_axes = ("zlo", "xhi")
    by_xor = jnp.stack(
        [attention]
        + [lax.ppermute(attention, quad_axes, [(i, i ^ m) for i in range(quad)]) for m in range(1, quad)]
    )
    mine = lax.axis_index(quad_axes)
    slab = jnp.concatenate(
        [lax.dynamic_index_in_dim(by_xor, q ^ mine, 0, keepdims=False) for q in range(quad)], axis=1
    )
    blocks = lax.all_gather(ring_block(out_weight), GROUP, axis=0).reshape(ring, quad, heads, -1)
    partial = jnp.einsum(
        "iqh,rqhf->irf", slab.reshape(-1, quad, heads), blocks, preferred_element_type=jnp.float32
    )
    received = lax.all_to_all(partial.astype(jnp.bfloat16), "zhi", 1, 1, tiled=True)
    summed = jnp.sum(received.astype(jnp.float32), axis=1)
    hidden = residual.astype(jnp.float32) + summed
    squares = jnp.sum(hidden * hidden, axis=1)
    for axis, mask in (("xhi", 1), ("zlo", 1), ("zhi", 1), ("zhi", 2)):
        size = lax.axis_size(axis)
        squares = squares + lax.ppermute(squares, axis, [(i, i ^ mask) for i in range(size)])
    normed = (hidden * lax.rsqrt(squares[:, None] / D + 1e-05) * gain[None, :]).astype(jnp.bfloat16)
    member = jnp.arange(R_DEV, dtype=jnp.int32)[:, None] == token_tr[0][None, :]
    counts = jnp.sum(member.astype(jnp.float32), axis=1, keepdims=True)
    binned = (
        jnp.dot(member.astype(jnp.bfloat16), normed, preferred_element_type=jnp.float32) / counts
    ).astype(jnp.bfloat16)
    width = binned.shape[1]
    total_trs = responses.shape[0]
    story = lax.all_gather(binned, GROUP, axis=0, tiled=True)
    extended = jnp.concatenate([jnp.zeros((LAGS, width), story.dtype), story], axis=0)
    contract = (((0,), (0,)), ((), ()))
    products = []
    for step in range(LAGS):
        start = LAGS - lag_offsets[step]
        lagged = lax.dynamic_slice_in_dim(extended, start, total_trs, 0)
        products.append(lax.dot_general(lagged, responses, contract, preferred_element_type=jnp.float32))
    scaled = jnp.stack(products) * (1.0 / jnp.sqrt(jnp.float32(total_trs)))
    return scaled.reshape(LAGS, width, responses.shape[1])


def solution(mesh):
    parts = Mesh(mesh.devices.reshape(2, 4, 2, 4, 2, 2), GROUP + TENSOR)
    return jax.shard_map(
        on_device,
        mesh=parts,
        in_specs=(
            P(GROUP, TENSOR),
            P(TENSOR, GROUP),
            P(GROUP, TENSOR),
            P(TENSOR),
            P(GROUP, None),
            P(),
            P(None, GROUP),
        ),
        out_specs=P(None, TENSOR, GROUP),
        check_vma=False,
    )
```

```python
import jax
import jax.numpy as jnp
from jax import lax
from jax.sharding import Mesh, PartitionSpec as P

D = 8192
LAGS = 4
R_DEV = 96
GROUP = ("xlo", "y", "core")
TENSOR = ("zhi", "zlo", "xhi")


def ring_block(block):
    groups = lax.axis_size(GROUP)
    tensors = lax.axis_size(TENSOR)
    quad = lax.axis_size(("zlo", "xhi"))
    route = []
    for g in range(groups):
        for t in range(tensors):
            ring, q = t // quad, t % quad
            source = (quad * (g // quad) + q) * tensors + quad * ring + g % quad
            route.append((source, g * tensors + t))
    return lax.ppermute(block, GROUP + TENSOR, route)


def on_device(attention, out_weight, residual, gain, token_tr, lag_offsets, responses):
    quad = lax.axis_size(("zlo", "xhi"))
    ring = lax.axis_size("zhi")
    heads = attention.shape[1]
    pair = lax.all_gather(attention, "xhi", axis=1, tiled=True)
    other = lax.ppermute(pair, "zlo", [(0, 1), (1, 0)])
    low = lax.axis_index("zlo") == 0
    slab = jnp.concatenate([jnp.where(low, pair, other), jnp.where(low, other, pair)], axis=1)
    blocks = lax.all_gather(ring_block(out_weight), GROUP, axis=0).reshape(ring, quad, heads, -1)
    partial = jnp.einsum(
        "iqh,rqhf->irf", slab.reshape(-1, quad, heads), blocks, preferred_element_type=jnp.float32
    )
    received = lax.all_to_all(partial.astype(jnp.bfloat16), "zhi", 1, 1, tiled=True)
    kept = (jnp.arange(ring) == lax.axis_index("zhi"))[None, :, None]
    summed = jnp.sum(jnp.where(kept, partial, received.astype(jnp.float32)), axis=1)
    hidden = residual.astype(jnp.float32) + summed
    squares = jnp.sum(hidden * hidden, axis=1)
    for axis, mask in (("xhi", 1), ("zlo", 1), ("zhi", 1), ("zhi", 2)):
        size = lax.axis_size(axis)
        squares = squares + lax.ppermute(squares, axis, [(i, i ^ mask) for i in range(size)])
    normed = (hidden * lax.rsqrt(squares[:, None] / D + 1e-05) * gain[None, :]).astype(jnp.bfloat16)
    member = jnp.arange(R_DEV, dtype=jnp.int32)[:, None] == token_tr[0][None, :]
    counts = jnp.sum(member.astype(jnp.float32), axis=1, keepdims=True)
    binned = (
        jnp.dot(member.astype(jnp.bfloat16), normed, preferred_element_type=jnp.float32) / counts
    ).astype(jnp.bfloat16)
    width = binned.shape[1]
    total_trs = responses.shape[0]
    story = lax.all_gather(binned, GROUP, axis=0, tiled=True)
    extended = jnp.concatenate([jnp.zeros((LAGS, width), story.dtype), story], axis=0)
    contract = (((0,), (0,)), ((), ()))
    products = []
    for step in range(LAGS):
        start = LAGS - lag_offsets[step]
        lagged = lax.dynamic_slice_in_dim(extended, start, total_trs, 0)
        products.append(lax.dot_general(lagged, responses, contract, preferred_element_type=jnp.float32))
    scaled = jnp.stack(products) * (1.0 / jnp.sqrt(jnp.float32(total_trs)))
    return scaled.reshape(LAGS, width, responses.shape[1])


def solution(mesh):
    parts = Mesh(mesh.devices.reshape(2, 4, 2, 4, 2, 2), GROUP + TENSOR)
    return jax.shard_map(
        on_device,
        mesh=parts,
        in_specs=(
            P(GROUP, TENSOR),
            P(TENSOR, GROUP),
            P(GROUP, TENSOR),
            P(TENSOR),
            P(GROUP, None),
            P(),
            P(None, GROUP),
        ),
        out_specs=P(None, TENSOR, GROUP),
        check_vma=False,
    )
```

```python
import jax
import jax.numpy as jnp
from jax import lax
from jax.sharding import Mesh, PartitionSpec as P

D = 8192
LAGS = 4
R_DEV = 96
GROUP = ("xlo", "y", "core")
TENSOR = ("zhi", "zlo", "xhi")


def ring_block(block):
    groups = lax.axis_size(GROUP)
    tensors = lax.axis_size(TENSOR)
    quad = lax.axis_size(("zlo", "xhi"))
    route = []
    for g in range(groups):
        for t in range(tensors):
            ring, q = t // quad, t % quad
            source = (quad * (g // quad) + q) * tensors + quad * ring + g % quad
            route.append((source, g * tensors + t))
    return lax.ppermute(block, GROUP + TENSOR, route)


def on_device(attention, out_weight, residual, gain, token_tr, lag_offsets, responses):
    quad = lax.axis_size(("zlo", "xhi"))
    ring = lax.axis_size("zhi")
    heads = attention.shape[1]
    pair = lax.all_gather(attention, "xhi", axis=1, tiled=True)
    other = lax.ppermute(pair, "zlo", [(0, 1), (1, 0)])
    low = lax.axis_index("zlo") == 0
    slab = jnp.concatenate([jnp.where(low, pair, other), jnp.where(low, other, pair)], axis=1)
    blocks = lax.all_gather(ring_block(out_weight), GROUP, axis=0).reshape(ring, quad, heads, -1)
    partial = jnp.einsum(
        "iqh,rqhf->irf", slab.reshape(-1, quad, heads), blocks, preferred_element_type=jnp.float32
    )
    received = lax.all_to_all(partial.astype(jnp.bfloat16), "zhi", 1, 1, tiled=True)
    summed = jnp.sum(received.astype(jnp.float32), axis=1)
    hidden = residual.astype(jnp.float32) + summed
    squares = jnp.sum(hidden * hidden, axis=1)
    for axis in (("zlo", "xhi"), "zhi"):
        size = lax.axis_size(axis)
        others = [lax.ppermute(squares, axis, [(i, i ^ m) for i in range(size)]) for m in range(1, size)]
        squares = squares + sum(others)
    normed = (hidden * lax.rsqrt(squares[:, None] / D + 1e-05) * gain[None, :]).astype(jnp.bfloat16)
    member = jnp.arange(R_DEV, dtype=jnp.int32)[:, None] == token_tr[0][None, :]
    counts = jnp.sum(member.astype(jnp.float32), axis=1, keepdims=True)
    binned = (
        jnp.dot(member.astype(jnp.bfloat16), normed, preferred_element_type=jnp.float32) / counts
    ).astype(jnp.bfloat16)
    width = binned.shape[1]
    total_trs = responses.shape[0]
    story = lax.all_gather(binned, GROUP, axis=0, tiled=True)
    extended = jnp.concatenate([jnp.zeros((LAGS, width), story.dtype), story], axis=0)
    contract = (((0,), (0,)), ((), ()))
    products = []
    for step in range(LAGS):
        start = LAGS - lag_offsets[step]
        lagged = lax.dynamic_slice_in_dim(extended, start, total_trs, 0)
        products.append(lax.dot_general(lagged, responses, contract, preferred_element_type=jnp.float32))
    scaled = jnp.stack(products) * (1.0 / jnp.sqrt(jnp.float32(total_trs)))
    return scaled.reshape(LAGS, width, responses.shape[1])


def solution(mesh):
    parts = Mesh(mesh.devices.reshape(2, 4, 2, 4, 2, 2), GROUP + TENSOR)
    return jax.shard_map(
        on_device,
        mesh=parts,
        in_specs=(
            P(GROUP, TENSOR),
            P(TENSOR, GROUP),
            P(GROUP, TENSOR),
            P(TENSOR),
            P(GROUP, None),
            P(),
            P(None, GROUP),
        ),
        out_specs=P(None, TENSOR, GROUP),
        check_vma=False,
    )
```

```python
import jax
import jax.numpy as jnp
from jax import lax
from jax.sharding import Mesh, PartitionSpec as P

D = 8192
LAGS = 4
R_DEV = 96
GROUP = ("xlo", "y", "core")
TENSOR = ("zhi", "zlo", "xhi")


def ring_block(block):
    groups = lax.axis_size(GROUP)
    tensors = lax.axis_size(TENSOR)
    quad = lax.axis_size(("zlo", "xhi"))
    route = []
    for g in range(groups):
        for t in range(tensors):
            ring, q = t // quad, t % quad
            source = (quad * (g // quad) + q) * tensors + quad * ring + g % quad
            route.append((source, g * tensors + t))
    return lax.ppermute(block, GROUP + TENSOR, route)


def on_device(attention, out_weight, residual, gain, token_tr, lag_offsets, responses):
    quad = lax.axis_size(("zlo", "xhi"))
    ring = lax.axis_size("zhi")
    heads = attention.shape[1]
    pair = lax.all_gather(attention, "xhi", axis=1, tiled=True)
    other = lax.ppermute(pair, "zlo", [(0, 1), (1, 0)])
    low = lax.axis_index("zlo") == 0
    slab = jnp.concatenate([jnp.where(low, pair, other), jnp.where(low, other, pair)], axis=1)
    fetched = ring_block(out_weight)
    lhs = slab.reshape(-1, quad, heads)
    cut = fetched.shape[1] // 2
    sums = []
    for cols in (slice(0, cut), slice(cut, None)):
        blocks = lax.all_gather(fetched[:, cols], GROUP, axis=0).reshape(ring, quad, heads, -1)
        partial = jnp.einsum("iqh,rqhf->irf", lhs, blocks, preferred_element_type=jnp.float32)
        received = lax.all_to_all(partial.astype(jnp.bfloat16), "zhi", 1, 1, tiled=True)
        sums.append(jnp.sum(received.astype(jnp.float32), axis=1))
    summed = jnp.concatenate(sums, axis=1)
    hidden = residual.astype(jnp.float32) + summed
    squares = jnp.sum(hidden * hidden, axis=1)
    for axis in (("zlo", "xhi"), "zhi"):
        size = lax.axis_size(axis)
        others = [lax.ppermute(squares, axis, [(i, i ^ m) for i in range(size)]) for m in range(1, size)]
        squares = squares + sum(others)
    normed = (hidden * lax.rsqrt(squares[:, None] / D + 1e-05) * gain[None, :]).astype(jnp.bfloat16)
    member = jnp.arange(R_DEV, dtype=jnp.int32)[:, None] == token_tr[0][None, :]
    counts = jnp.sum(member.astype(jnp.float32), axis=1, keepdims=True)
    binned = (
        jnp.dot(member.astype(jnp.bfloat16), normed, preferred_element_type=jnp.float32) / counts
    ).astype(jnp.bfloat16)
    width = binned.shape[1]
    total_trs = responses.shape[0]
    story = lax.all_gather(binned, GROUP, axis=0, tiled=True)
    extended = jnp.concatenate([jnp.zeros((LAGS, width), story.dtype), story], axis=0)
    contract = (((0,), (0,)), ((), ()))
    products = []
    for step in range(LAGS):
        start = LAGS - lag_offsets[step]
        lagged = lax.dynamic_slice_in_dim(extended, start, total_trs, 0)
        products.append(lax.dot_general(lagged, responses, contract, preferred_element_type=jnp.float32))
    scaled = jnp.stack(products) * (1.0 / jnp.sqrt(jnp.float32(total_trs)))
    return scaled.reshape(LAGS, width, responses.shape[1])


def solution(mesh):
    parts = Mesh(mesh.devices.reshape(2, 4, 2, 4, 2, 2), GROUP + TENSOR)
    return jax.shard_map(
        on_device,
        mesh=parts,
        in_specs=(
            P(GROUP, TENSOR),
            P(TENSOR, GROUP),
            P(GROUP, TENSOR),
            P(TENSOR),
            P(GROUP, None),
            P(),
            P(None, GROUP),
        ),
        out_specs=P(None, TENSOR, GROUP),
        check_vma=False,
    )
```

```python
import jax
import jax.numpy as jnp
from jax import lax
from jax.sharding import Mesh, PartitionSpec as P

D = 8192
LAGS = 4
R_DEV = 96
GROUP = ("xlo", "y", "core")
TENSOR = ("zhi", "zlo", "xhi")


def ring_block(block):
    groups = lax.axis_size(GROUP)
    tensors = lax.axis_size(TENSOR)
    zlos, xs = lax.axis_size("zlo"), lax.axis_size("xhi")
    route = []
    for g in range(groups):
        for t in range(tensors):
            zhi, zlo, x = t // (zlos * xs), (t // xs) % zlos, t % xs
            r, q = g // (2 * xs), g % (2 * xs)
            feats = zhi * zlos * xs + r * xs + x
            heads = (q // xs) * zlos * xs + zlo * xs + q % xs
            route.append((feats * tensors + heads, g * tensors + t))
    return lax.ppermute(block, GROUP + TENSOR, route)


def on_device(attention, out_weight, residual, gain, token_tr, lag_offsets, responses):
    quad = lax.axis_size(("zhi", "xhi"))
    ring = lax.axis_size("zlo")
    heads = attention.shape[1]
    pair = lax.all_gather(attention, "xhi", axis=1, tiled=True)
    other = lax.ppermute(pair, "zhi", [(0, 1), (1, 0)])
    low = lax.axis_index("zhi") == 0
    slab = jnp.concatenate([jnp.where(low, pair, other), jnp.where(low, other, pair)], axis=1)
    blocks = lax.all_gather(ring_block(out_weight), GROUP, axis=0).reshape(ring, quad, heads, -1)
    partial = jnp.einsum(
        "iqh,rqhf->irf", slab.reshape(-1, quad, heads), blocks, preferred_element_type=jnp.float32
    )
    received = lax.all_to_all(partial.astype(jnp.bfloat16), "zlo", 1, 1, tiled=True)
    summed = jnp.sum(received.astype(jnp.float32), axis=1)
    hidden = residual.astype(jnp.float32) + summed
    squares = jnp.sum(hidden * hidden, axis=1)
    for axis in (("zhi", "xhi"), "zlo"):
        size = lax.axis_size(axis)
        others = [lax.ppermute(squares, axis, [(i, i ^ m) for i in range(size)]) for m in range(1, size)]
        squares = squares + sum(others)
    normed = (hidden * lax.rsqrt(squares[:, None] / D + 1e-05) * gain[None, :]).astype(jnp.bfloat16)
    member = jnp.arange(R_DEV, dtype=jnp.int32)[:, None] == token_tr[0][None, :]
    counts = jnp.sum(member.astype(jnp.float32), axis=1, keepdims=True)
    binned = (
        jnp.dot(member.astype(jnp.bfloat16), normed, preferred_element_type=jnp.float32) / counts
    ).astype(jnp.bfloat16)
    width = binned.shape[1]
    total_trs = responses.shape[0]
    story = lax.all_gather(binned, GROUP, axis=0, tiled=True)
    extended = jnp.concatenate([jnp.zeros((LAGS, width), story.dtype), story], axis=0)
    contract = (((0,), (0,)), ((), ()))
    products = []
    for step in range(LAGS):
        start = LAGS - lag_offsets[step]
        lagged = lax.dynamic_slice_in_dim(extended, start, total_trs, 0)
        products.append(lax.dot_general(lagged, responses, contract, preferred_element_type=jnp.float32))
    scaled = jnp.stack(products) * (1.0 / jnp.sqrt(jnp.float32(total_trs)))
    return scaled.reshape(LAGS, width, responses.shape[1])


def solution(mesh):
    parts = Mesh(mesh.devices.reshape(2, 4, 2, 2, 4, 2), GROUP + TENSOR)
    return jax.shard_map(
        on_device,
        mesh=parts,
        in_specs=(
            P(GROUP, TENSOR),
            P(TENSOR, GROUP),
            P(GROUP, TENSOR),
            P(TENSOR),
            P(GROUP, None),
            P(),
            P(None, GROUP),
        ),
        out_specs=P(None, TENSOR, GROUP),
        check_vma=False,
    )
```

```python
import jax
import jax.numpy as jnp
from jax import lax
from jax.sharding import Mesh, PartitionSpec as P

D = 8192
LAGS = 4
R_DEV = 96
GROUP = ("xlo", "y", "core")
TENSOR = ("zhi", "zlo", "xhi")


def ring_block(block):
    groups = lax.axis_size(GROUP)
    tensors = lax.axis_size(TENSOR)
    quad = lax.axis_size(("zlo", "xhi"))
    route = []
    for g in range(groups):
        for t in range(tensors):
            ring, q = t // quad, t % quad
            source = (quad * (g // quad) + q) * tensors + quad * ring + g % quad
            route.append((source, g * tensors + t))
    return lax.ppermute(block, GROUP + TENSOR, route)


def on_device(attention, out_weight, residual, gain, token_tr, lag_offsets, responses):
    quad = lax.axis_size(("zlo", "xhi"))
    ring = lax.axis_size("zhi")
    heads = attention.shape[1]
    pair = lax.all_gather(attention, "xhi", axis=1, tiled=True)
    other = lax.ppermute(pair, "zlo", [(0, 1), (1, 0)])
    low = lax.axis_index("zlo") == 0
    slab = jnp.concatenate([jnp.where(low, pair, other), jnp.where(low, other, pair)], axis=1)
    blocks = lax.all_gather(ring_block(out_weight), GROUP, axis=0).reshape(ring, quad, heads, -1)
    partial = jnp.einsum(
        "iqh,rqhf->irf", slab.reshape(-1, quad, heads), blocks, preferred_element_type=jnp.float32
    )
    received = lax.all_to_all(partial.astype(jnp.bfloat16), "zhi", 1, 1, tiled=True)
    summed = jnp.sum(received.astype(jnp.float32), axis=1)
    hidden = residual.astype(jnp.float32) + summed
    squares = jnp.sum(hidden * hidden, axis=1)
    for axis in (("zlo", "xhi"), "zhi"):
        size = lax.axis_size(axis)
        others = [lax.ppermute(squares, axis, [(i, i ^ m) for i in range(size)]) for m in range(1, size)]
        squares = squares + sum(others)
    normed = (hidden * lax.rsqrt(squares[:, None] / D + 1e-05) * gain[None, :]).astype(jnp.bfloat16)
    member = jnp.arange(R_DEV, dtype=jnp.int32)[:, None] == token_tr[0][None, :]
    counts = jnp.sum(member.astype(jnp.float32), axis=1, keepdims=True)
    binned = (
        jnp.dot(member.astype(jnp.bfloat16), normed, preferred_element_type=jnp.float32) / counts
    ).astype(jnp.bfloat16)
    width = binned.shape[1]
    total_trs = responses.shape[0]
    story = binned[None]
    for axis in ("y", ("xlo", "core")):
        size = lax.axis_size(axis)
        by_xor = jnp.stack(
            [story] + [lax.ppermute(story, axis, [(i, i ^ m) for i in range(size)]) for m in range(1, size)]
        )
        mine = lax.axis_index(axis)
        story = jnp.stack([lax.dynamic_index_in_dim(by_xor, p ^ mine, 0, keepdims=False) for p in range(size)])
    xlos, ys, cores = lax.axis_size("xlo"), lax.axis_size("y"), lax.axis_size("core")
    story = story.reshape(xlos, cores, ys, -1, width).transpose(0, 2, 1, 3, 4).reshape(-1, width)
    extended = jnp.concatenate([jnp.zeros((LAGS, width), story.dtype), story], axis=0)
    contract = (((0,), (0,)), ((), ()))
    products = []
    for step in range(LAGS):
        start = LAGS - lag_offsets[step]
        lagged = lax.dynamic_slice_in_dim(extended, start, total_trs, 0)
        products.append(lax.dot_general(lagged, responses, contract, preferred_element_type=jnp.float32))
    scaled = jnp.stack(products) * (1.0 / jnp.sqrt(jnp.float32(total_trs)))
    return scaled.reshape(LAGS, width, responses.shape[1])


def solution(mesh):
    parts = Mesh(mesh.devices.reshape(2, 4, 2, 4, 2, 2), GROUP + TENSOR)
    return jax.shard_map(
        on_device,
        mesh=parts,
        in_specs=(
            P(GROUP, TENSOR),
            P(TENSOR, GROUP),
            P(GROUP, TENSOR),
            P(TENSOR),
            P(GROUP, None),
            P(),
            P(None, GROUP),
        ),
        out_specs=P(None, TENSOR, GROUP),
        check_vma=False,
    )
```

```python
import jax
import jax.numpy as jnp
from jax import lax
from jax.sharding import Mesh, PartitionSpec as P

D = 8192
LAGS = 4
R_DEV = 96
GROUP = ("xlo", "y", "core")
TENSOR = ("zhi", "zlo", "xhi")


def ring_block(block):
    groups = lax.axis_size(GROUP)
    tensors = lax.axis_size(TENSOR)
    quad = lax.axis_size(("zlo", "xhi"))
    route = []
    for g in range(groups):
        for t in range(tensors):
            ring, q = t // quad, t % quad
            source = (quad * (g // quad) + q) * tensors + quad * ring + g % quad
            route.append((source, g * tensors + t))
    return lax.ppermute(block, GROUP + TENSOR, route)


def gather_group(block):
    gathered = block[None]
    for axis in ("y", ("xlo", "core")):
        size = lax.axis_size(axis)
        by_xor = jnp.stack(
            [gathered] + [lax.ppermute(gathered, axis, [(i, i ^ m) for i in range(size)]) for m in range(1, size)]
        )
        mine = lax.axis_index(axis)
        gathered = jnp.stack([lax.dynamic_index_in_dim(by_xor, p ^ mine, 0, keepdims=False) for p in range(size)])
    xlos, ys, cores = lax.axis_size("xlo"), lax.axis_size("y"), lax.axis_size("core")
    shape = block.shape
    return gathered.reshape((xlos, cores, ys) + shape).transpose((0, 2, 1) + tuple(range(3, 3 + len(shape)))).reshape((-1,) + shape)


def on_device(attention, out_weight, residual, gain, token_tr, lag_offsets, responses):
    quad = lax.axis_size(("zlo", "xhi"))
    ring = lax.axis_size("zhi")
    heads = attention.shape[1]
    pair = lax.all_gather(attention, "xhi", axis=1, tiled=True)
    other = lax.ppermute(pair, "zlo", [(0, 1), (1, 0)])
    low = lax.axis_index("zlo") == 0
    slab = jnp.concatenate([jnp.where(low, pair, other), jnp.where(low, other, pair)], axis=1)
    blocks = gather_group(ring_block(out_weight)).reshape(ring, quad, heads, -1)
    partial = jnp.einsum(
        "iqh,rqhf->irf", slab.reshape(-1, quad, heads), blocks, preferred_element_type=jnp.float32
    )
    received = lax.all_to_all(partial.astype(jnp.bfloat16), "zhi", 1, 1, tiled=True)
    summed = jnp.sum(received.astype(jnp.float32), axis=1)
    hidden = residual.astype(jnp.float32) + summed
    squares = jnp.sum(hidden * hidden, axis=1)
    for axis in (("zlo", "xhi"), "zhi"):
        size = lax.axis_size(axis)
        others = [lax.ppermute(squares, axis, [(i, i ^ m) for i in range(size)]) for m in range(1, size)]
        squares = squares + sum(others)
    normed = (hidden * lax.rsqrt(squares[:, None] / D + 1e-05) * gain[None, :]).astype(jnp.bfloat16)
    member = jnp.arange(R_DEV, dtype=jnp.int32)[:, None] == token_tr[0][None, :]
    counts = jnp.sum(member.astype(jnp.float32), axis=1, keepdims=True)
    binned = (
        jnp.dot(member.astype(jnp.bfloat16), normed, preferred_element_type=jnp.float32) / counts
    ).astype(jnp.bfloat16)
    width = binned.shape[1]
    total_trs = responses.shape[0]
    story = gather_group(binned).reshape(-1, width)
    extended = jnp.concatenate([jnp.zeros((LAGS, width), story.dtype), story], axis=0)
    contract = (((0,), (0,)), ((), ()))
    products = []
    for step in range(LAGS):
        start = LAGS - lag_offsets[step]
        lagged = lax.dynamic_slice_in_dim(extended, start, total_trs, 0)
        products.append(lax.dot_general(lagged, responses, contract, preferred_element_type=jnp.float32))
    scaled = jnp.stack(products) * (1.0 / jnp.sqrt(jnp.float32(total_trs)))
    return scaled.reshape(LAGS, width, responses.shape[1])


def solution(mesh):
    parts = Mesh(mesh.devices.reshape(2, 4, 2, 4, 2, 2), GROUP + TENSOR)
    return jax.shard_map(
        on_device,
        mesh=parts,
        in_specs=(
            P(GROUP, TENSOR),
            P(TENSOR, GROUP),
            P(GROUP, TENSOR),
            P(TENSOR),
            P(GROUP, None),
            P(),
            P(None, GROUP),
        ),
        out_specs=P(None, TENSOR, GROUP),
        check_vma=False,
    )
```

```python
import jax
import jax.numpy as jnp
from jax import lax
from jax.sharding import Mesh, PartitionSpec as P

D = 8192
LAGS = 4
R_DEV = 96
GROUP = ("xlo", "y", "core")
TENSOR = ("zhi", "zlo", "xhi")


def ring_block(block):
    groups = lax.axis_size(GROUP)
    tensors = lax.axis_size(TENSOR)
    quad = lax.axis_size(("zlo", "xhi"))
    route = []
    for g in range(groups):
        for t in range(tensors):
            ring, q = t // quad, t % quad
            source = (quad * (g // quad) + q) * tensors + quad * ring + g % quad
            route.append((source, g * tensors + t))
    return lax.ppermute(block, GROUP + TENSOR, route)


def on_device(attention, out_weight, residual, gain, token_tr, lag_offsets, responses):
    quad = lax.axis_size(("zlo", "xhi"))
    ring = lax.axis_size("zhi")
    heads = attention.shape[1]
    partner = lax.ppermute(attention, "xhi", [(0, 1), (1, 0)])
    first = lax.axis_index("xhi") == 0
    pair = jnp.concatenate([jnp.where(first, attention, partner), jnp.where(first, partner, attention)], axis=1)
    other = lax.ppermute(pair, "zlo", [(0, 1), (1, 0)])
    low = lax.axis_index("zlo") == 0
    slab = jnp.concatenate([jnp.where(low, pair, other), jnp.where(low, other, pair)], axis=1)
    blocks = lax.all_gather(ring_block(out_weight), GROUP, axis=0).reshape(ring, quad, heads, -1)
    partial = jnp.einsum(
        "iqh,rqhf->irf", slab.reshape(-1, quad, heads), blocks, preferred_element_type=jnp.float32
    )
    received = lax.all_to_all(partial.astype(jnp.bfloat16), "zhi", 1, 1, tiled=True)
    summed = jnp.sum(received.astype(jnp.float32), axis=1)
    hidden = residual.astype(jnp.float32) + summed
    squares = jnp.sum(hidden * hidden, axis=1)
    for axis in (("zlo", "xhi"), "zhi"):
        size = lax.axis_size(axis)
        others = [lax.ppermute(squares, axis, [(i, i ^ m) for i in range(size)]) for m in range(1, size)]
        squares = squares + sum(others)
    normed = (hidden * lax.rsqrt(squares[:, None] / D + 1e-05) * gain[None, :]).astype(jnp.bfloat16)
    member = jnp.arange(R_DEV, dtype=jnp.int32)[:, None] == token_tr[0][None, :]
    counts = jnp.sum(member.astype(jnp.float32), axis=1, keepdims=True)
    binned = (
        jnp.dot(member.astype(jnp.bfloat16), normed, preferred_element_type=jnp.float32) / counts
    ).astype(jnp.bfloat16)
    width = binned.shape[1]
    total_trs = responses.shape[0]
    story = binned[None]
    for axis in ("y", ("xlo", "core")):
        size = lax.axis_size(axis)
        by_xor = jnp.stack(
            [story] + [lax.ppermute(story, axis, [(i, i ^ m) for i in range(size)]) for m in range(1, size)]
        )
        mine = lax.axis_index(axis)
        story = jnp.stack([lax.dynamic_index_in_dim(by_xor, p ^ mine, 0, keepdims=False) for p in range(size)])
    xlos, ys, cores = lax.axis_size("xlo"), lax.axis_size("y"), lax.axis_size("core")
    story = story.reshape(xlos, cores, ys, -1, width).transpose(0, 2, 1, 3, 4).reshape(-1, width)
    extended = jnp.concatenate([jnp.zeros((LAGS, width), story.dtype), story], axis=0)
    contract = (((0,), (0,)), ((), ()))
    products = []
    for step in range(LAGS):
        start = LAGS - lag_offsets[step]
        lagged = lax.dynamic_slice_in_dim(extended, start, total_trs, 0)
        products.append(lax.dot_general(lagged, responses, contract, preferred_element_type=jnp.float32))
    scaled = jnp.stack(products) * (1.0 / jnp.sqrt(jnp.float32(total_trs)))
    return scaled.reshape(LAGS, width, responses.shape[1])


def solution(mesh):
    parts = Mesh(mesh.devices.reshape(2, 4, 2, 4, 2, 2), GROUP + TENSOR)
    return jax.shard_map(
        on_device,
        mesh=parts,
        in_specs=(
            P(GROUP, TENSOR),
            P(TENSOR, GROUP),
            P(GROUP, TENSOR),
            P(TENSOR),
            P(GROUP, None),
            P(),
            P(None, GROUP),
        ),
        out_specs=P(None, TENSOR, GROUP),
        check_vma=False,
    )
```
